256 devices in a mesh: opair: 8 (over y, core), vpair: 32 (over z, x).
Axes of the slice: x: 4, y: 4, z: 8, core: 2. Of those that a mesh axis runs over, the one named last changes fastest.
Arguments:
- amplitudes: bfloat16 [1600, 24, 1000], P('vpair', 'opair'), may hold values from -6 to 6
- ladder_ints: bfloat16 [24, 1000, 32, 1000], P('opair', None, 'vpair'), may hold values from -0.0390625 to 0.0390625
- cycle_amps: bfloat16 [24, 100, 512], P('opair'), may hold values from -6 to 6
- cycle_ints: bfloat16 [24, 100, 100000], P('opair', None, 'vpair'), may hold values from -0.125 to 0.125
- occ_blocks: int32 [8], replicated, may hold values from 1 to 33, 100 in all
- virt_blocks: int32 [8], replicated, may hold values from 1 to 250, 1000 in all
- occ_start: int32 [1], replicated, may hold values from 0 to 84
- virt_start: int32 [1], replicated, may hold values from 0 to 968
- eps_occ: float32 [100], replicated, may hold values from -1 to -0.25
- eps_virt: float32 [1000], replicated, may hold values from 0.25 to 1.5
Outputs:
- update: float32 [16, 32, 100, 1000], P('opair', 'vpair')
The draws below stay inside these ranges and needn't reach their ends.
All inputs are finite; a program needn't handle non-finite values.
Results may differ from the reference program's by a relative error of at most 0.0004.
Values may be sent and summed in bfloat16 or wider, within the bound.
No kernel may reach another device: no remote copies, remote signals or barrier semaphores. Data moves between devices by JAX's collectives and lax.ppermute only.
A program may use at most 128 MiB of HBM per device.

```python
import math
import jax
import jax.numpy as jnp
import numpy as np
from jax import lax

NO = 100
NV = 1000
I_WIN = 16
A_WIN = 32
C_WIN = 24
PAIRS = 1600


def level_of(own_key, shape, pieces, low, top_value):
    loudness = 1.0
    for axis_at, parts in pieces:
        draws = jax.random.uniform(jax.random.fold_in(jax.random.fold_in(own_key, 6), axis_at), (parts,), jnp.float32, low / len(pieces), top_value / len(pieces))
        loudness = loudness * jnp.repeat(jnp.exp(draws), shape[axis_at] // parts).reshape((-1,) + (1,) * (len(shape) - 1 - axis_at))
    return loudness


def split_up(amount, total, bound, lean):
    loads = [(1 << 20) // math.isqrt(standing ** lean) + 1 for standing in range(2, amount + 1)]
    rest, holding = total - bound - (amount - 1), [1] * (amount - 1)
    while rest > 0:
        movable = [i for i in range(amount - 1) if holding[i] < bound]
        pool, left = sum([loads[i] for i in movable]), rest
        for i in movable:
            more = min(bound - holding[i], max(1, left * loads[i] // pool), rest)
            holding[i] = holding[i] + more
            rest = rest - more
    return np.array([bound] + holding)


def ragged(own_key, number_of, total, bound, slope):
    if number_of == 2:
        one = jax.random.randint(own_key, (), max(1, total - bound), min(bound, total - 1) + 1)
        return jnp.stack([one, total - one])
    lengths = jnp.asarray(split_up(number_of, total, bound, slope), jnp.int32)
    couples = (number_of - 1) // 2
    giver, sink = lengths[1:1 + 2 * couples:2], lengths[2:2 + 2 * couples:2]
    margin = jnp.minimum(giver - 1, bound - sink)
    shifted = jax.random.randint(jax.random.fold_in(own_key, 1), (couples,), 0, 1 << 20) % (margin + 1)
    lengths = lengths.at[1:1 + 2 * couples:2].set(giver - shifted).at[2:2 + 2 * couples:2].set(sink + shifted)
    return lengths[jax.random.permutation(jax.random.fold_in(own_key, 2), number_of)]


def normal_values(key, extent, deviation, reach, cuts=(), kind=jnp.bfloat16):
    array = deviation * jax.random.normal(key, extent, jnp.float32)
    if cuts:
        array = array * level_of(key, extent, cuts, -0.22, 0.18)
    return jnp.clip(array, -reach, reach).astype(kind)


def setup_inputs(seed: int = 0) -> dict:
    splits = jax.random.split(jax.random.key(seed), 11)
    return {
        "amplitudes": normal_values(splits[0], (PAIRS, C_WIN, NV), 1.0, 6.0, ((0, 32), (1, 8))),
        "ladder_ints": normal_values(splits[1], (C_WIN, NV, A_WIN, NV), (C_WIN * NV) ** -0.5, 0.0390625, ((0, 8), (2, 32))),
        "cycle_amps": normal_values(splits[2], (C_WIN, NO, I_WIN * A_WIN), 1.0, 6.0, ((0, 8),)),
        "cycle_ints": normal_values(splits[3], (C_WIN, NO, NO * NV), (C_WIN * NO) ** -0.5, 0.125, ((0, 8), (2, 32))),
        "occ_blocks": ragged(splits[4], 8, NO, NO // 3, 2).astype(jnp.int32),
        "virt_blocks": ragged(splits[5], 8, NV, NV // 4, 2).astype(jnp.int32),
        "occ_start": jax.random.randint(splits[6], (1,), 0, NO - I_WIN + 1).astype(jnp.int32),
        "virt_start": jax.random.randint(splits[7], (1,), 0, NV - A_WIN + 1).astype(jnp.int32),
        "eps_occ": jnp.clip(jax.random.uniform(splits[8], (NO,), jnp.float32, -1.0, -0.25), -1.0, -0.25),
        "eps_virt": jnp.clip(jax.random.uniform(splits[9], (NV,), jnp.float32, 0.25, 1.5), 0.25, 1.5),
    }


def irrep_of(blocks, index):
    bounds = jnp.cumsum(blocks)[:-1]
    return jnp.sum((index[:, None] >= bounds[None, :]).astype(jnp.int32), axis=1)


def reference(amplitudes, ladder_ints, cycle_amps, cycle_ints, occ_blocks, virt_blocks, occ_start, virt_start, eps_occ, eps_virt):
    def accumulate(carry, slab):
        ladder, cycle = carry
        t_slab = lax.dynamic_index_in_dim(amplitudes, slab, 1, keepdims=False)
        v_slab = lax.dynamic_index_in_dim(ladder_ints, slab, 0, keepdims=False).reshape(NV, A_WIN * NV)
        ladder = ladder + jnp.dot(t_slab, v_slab, preferred_element_type=jnp.float32)
        x_slab = lax.dynamic_index_in_dim(cycle_amps, slab, 0, keepdims=False)
        y_slab = lax.dynamic_index_in_dim(cycle_ints, slab, 0, keepdims=False)
        cycle = cycle + jnp.dot(x_slab.T, y_slab, preferred_element_type=jnp.float32)
        return (ladder, cycle), None

    start = (jnp.zeros((PAIRS, A_WIN * NV), jnp.float32), jnp.zeros((I_WIN * A_WIN, NO * NV), jnp.float32))
    (ladder, cycle), _ = lax.scan(accumulate, start, jnp.arange(C_WIN, dtype=jnp.int32))
    ladder = ladder.reshape(I_WIN, NO, A_WIN, NV).transpose(0, 2, 1, 3)
    resid = ladder + cycle.reshape(I_WIN, A_WIN, NO, NV)
    first_occ = occ_start[0].astype(jnp.int32)
    first_virt = virt_start[0].astype(jnp.int32)
    glob_i = first_occ + jnp.arange(I_WIN, dtype=jnp.int32)
    glob_a = first_virt + jnp.arange(A_WIN, dtype=jnp.int32)
    sym_i = irrep_of(occ_blocks, glob_i)
    sym_a = irrep_of(virt_blocks, glob_a)
    sym_j = irrep_of(occ_blocks, jnp.arange(NO, dtype=jnp.int32))
    sym_b = irrep_of(virt_blocks, jnp.arange(NV, dtype=jnp.int32))
    total_sym = jnp.bitwise_xor(jnp.bitwise_xor(sym_i[:, None, None, None], sym_a[None, :, None, None]), jnp.bitwise_xor(sym_j[None, None, :, None], sym_b[None, None, None, :]))
    e_i = lax.dynamic_slice_in_dim(eps_occ, first_occ, I_WIN)
    e_a = lax.dynamic_slice_in_dim(eps_virt, first_virt, A_WIN)
    denom = e_i[:, None, None, None] - e_a[None, :, None, None] + eps_occ[None, None, :, None] - eps_virt[None, None, None, :]
    return jnp.where(total_sym == 0, resid / denom, jnp.float32(0.0))
```

```python
import jax
import jax.numpy as jnp
from jax import lax
from jax.sharding import PartitionSpec as P

NO = 100
NV = 1000
I_DEV = 2
A_DEV = 1


def irrep_of(blocks, index):
    bounds = jnp.cumsum(blocks)[:-1]
    return jnp.sum((index[:, None] >= bounds[None, :]).astype(jnp.int32), axis=1)


def shards(
    amplitudes,
    ladder_ints,
    cycle_amps,
    cycle_ints,
    occ_blocks,
    virt_blocks,
    occ_start,
    virt_start,
    eps_occ,
    eps_virt,
):
    i_win = I_DEV * lax.axis_size("opair")
    a_win = A_DEV * lax.axis_size("vpair")
    slab_depth = ladder_ints.shape[0] * ladder_ints.shape[1]
    jb_dev = cycle_ints.shape[2]
    cycle = lax.dot_general(
        cycle_amps, cycle_ints, (((0, 1), (0, 1)), ((), ())), preferred_element_type=jnp.float32
    )
    cycle = cycle.reshape(i_win, a_win, jb_dev)
    cycle = lax.psum_scatter(cycle, "opair", scatter_dimension=0, tiled=True)
    cycle = lax.all_to_all(cycle, "vpair", split_axis=1, concat_axis=2, tiled=True)
    ladder_flat = ladder_ints.reshape(slab_depth, A_DEV * NV)
    piece = lax.all_gather(amplitudes, "vpair", axis=0, tiled=True)
    ladder = jnp.dot(
        piece.reshape(piece.shape[0], slab_depth), ladder_flat, preferred_element_type=jnp.float32
    )
    ladder = ladder.reshape(i_win, NO, A_DEV * NV)
    ladder, cycle = lax.optimization_barrier((ladder, cycle))
    ladder = lax.psum_scatter(ladder, "opair", scatter_dimension=0, tiled=True)
    resid = ladder.reshape(I_DEV, NO, A_DEV, NV).transpose(0, 2, 1, 3) + cycle.reshape(
        I_DEV, A_DEV, NO, NV
    )
    first_occ = occ_start[0] + lax.axis_index("opair") * I_DEV
    first_virt = virt_start[0] + lax.axis_index("vpair") * A_DEV
    glob_i = first_occ + jnp.arange(I_DEV, dtype=jnp.int32)
    glob_a = first_virt + jnp.arange(A_DEV, dtype=jnp.int32)
    sym_i = irrep_of(occ_blocks, glob_i)
    sym_a = irrep_of(virt_blocks, glob_a)
    sym_j = irrep_of(occ_blocks, jnp.arange(NO, dtype=jnp.int32))
    sym_b = irrep_of(virt_blocks, jnp.arange(NV, dtype=jnp.int32))
    total_sym = jnp.bitwise_xor(
        jnp.bitwise_xor(sym_i[:, None, None, None], sym_a[None, :, None, None]),
        jnp.bitwise_xor(sym_j[None, None, :, None], sym_b[None, None, None, :]),
    )
    e_i = lax.dynamic_slice_in_dim(eps_occ, first_occ, I_DEV)
    e_a = lax.dynamic_slice_in_dim(eps_virt, first_virt, A_DEV)
    denom = (
        e_i[:, None, None, None]
        - e_a[None, :, None, None]
        + eps_occ[None, None, :, None]
        - eps_virt[None, None, None, :]
    )
    return jnp.where(total_sym == 0, resid / denom, jnp.float32(0.0))


def solution(mesh):
    placed = (
        P("vpair", "opair", None),
        P("opair", None, "vpair", None),
        P("opair", None, None),
        P("opair", None, "vpair"),
        P(),
        P(),
        P(),
        P(),
        P(),
        P(),
    )
    return jax.shard_map(
        shards,
        mesh=mesh,
        in_specs=placed,
        out_specs=P("opair", "vpair", None, None),
        check_vma=False,
    )
```

```python
import jax
import jax.numpy as jnp
from jax import lax
from jax.sharding import PartitionSpec as P

NO = 100
NV = 1000
I_DEV = 2
A_DEV = 1
N_CHUNK = 2


def irrep_of(blocks, index):
    bounds = jnp.cumsum(blocks)[:-1]
    return jnp.sum((index[:, None] >= bounds[None, :]).astype(jnp.int32), axis=1)


def shards(
    amplitudes,
    ladder_ints,
    cycle_amps,
    cycle_ints,
    occ_blocks,
    virt_blocks,
    occ_start,
    virt_start,
    eps_occ,
    eps_virt,
):
    i_win = I_DEV * lax.axis_size("opair")
    a_win = A_DEV * lax.axis_size("vpair")
    slab_depth = ladder_ints.shape[0] * ladder_ints.shape[1]
    jb_dev = cycle_ints.shape[2]
    cycle = lax.dot_general(
        cycle_amps, cycle_ints, (((0, 1), (0, 1)), ((), ())), preferred_element_type=jnp.float32
    )
    cycle_part = cycle.reshape(i_win, a_win, jb_dev)
    c_dev = ladder_ints.shape[0]
    v_slab = ladder_ints.reshape(c_dev, ladder_ints.shape[1], A_DEV * NV)
    p_dev = amplitudes.shape[0]
    p_chunk = p_dev // N_CHUNK
    parts = []
    prev = None
    for s in range(N_CHUNK):
        loc = amplitudes[s * p_chunk : (s + 1) * p_chunk].transpose(1, 0, 2)
        if prev is None:
            loc, cycle_part = lax.optimization_barrier((loc, cycle_part))
            cycle = lax.psum_scatter(cycle_part, "opair", scatter_dimension=0, tiled=True)
        elif s == 1:
            loc, _, cycle = lax.optimization_barrier((loc, prev, cycle))
        else:
            loc, _ = lax.optimization_barrier((loc, prev))
        piece = lax.all_gather(loc, "vpair", axis=1, tiled=True)
        prev = piece
        part = lax.dot_general(
            piece, v_slab, (((0, 2), (0, 1)), ((), ())), preferred_element_type=jnp.float32
        )
        part = part.reshape(i_win, NO // N_CHUNK, A_DEV * NV)
        if s == 1:
            cycle = lax.all_to_all(cycle, "vpair", split_axis=1, concat_axis=2, tiled=True)
            part, parts[-1], cycle = lax.optimization_barrier((part, parts[-1], cycle))
        elif parts:
            part, parts[-1] = lax.optimization_barrier((part, parts[-1]))
        parts.append(lax.psum_scatter(part, "opair", scatter_dimension=0, tiled=True))
    parts = [q.reshape(I_DEV, NO // p_dev, p_chunk, A_DEV * NV) for q in parts]
    ladder = jnp.stack(parts, axis=2).reshape(I_DEV, NO, A_DEV * NV)
    resid = ladder.reshape(I_DEV, NO, A_DEV, NV).transpose(0, 2, 1, 3) + cycle.reshape(
        I_DEV, A_DEV, NO, NV
    )
    first_occ = occ_start[0] + lax.axis_index("opair") * I_DEV
    first_virt = virt_start[0] + lax.axis_index("vpair") * A_DEV
    glob_i = first_occ + jnp.arange(I_DEV, dtype=jnp.int32)
    glob_a = first_virt + jnp.arange(A_DEV, dtype=jnp.int32)
    sym_i = irrep_of(occ_blocks, glob_i)
    sym_a = irrep_of(virt_blocks, glob_a)
    sym_j = irrep_of(occ_blocks, jnp.arange(NO, dtype=jnp.int32))
    sym_b = irrep_of(virt_blocks, jnp.arange(NV, dtype=jnp.int32))
    total_sym = jnp.bitwise_xor(
        jnp.bitwise_xor(sym_i[:, None, None, None], sym_a[None, :, None, None]),
        jnp.bitwise_xor(sym_j[None, None, :, None], sym_b[None, None, None, :]),
    )
    e_i = lax.dynamic_slice_in_dim(eps_occ, first_occ, I_DEV)
    e_a = lax.dynamic_slice_in_dim(eps_virt, first_virt, A_DEV)
    denom = (
        e_i[:, None, None, None]
        - e_a[None, :, None, None]
        + eps_occ[None, None, :, None]
        - eps_virt[None, None, None, :]
    )
    return jnp.where(total_sym == 0, resid / denom, jnp.float32(0.0))


def solution(mesh):
    placed = (
        P("vpair", "opair", None),
        P("opair", None, "vpair", None),
        P("opair", None, None),
        P("opair", None, "vpair"),
        P(),
        P(),
        P(),
        P(),
        P(),
        P(),
    )
    return jax.shard_map(
        shards,
        mesh=mesh,
        in_specs=placed,
        out_specs=P("opair", "vpair", None, None),
        check_vma=False,
    )
```

```python
import jax
import jax.numpy as jnp
from jax import lax
from jax.sharding import PartitionSpec as P

NO = 100
NV = 1000
I_DEV = 2
A_DEV = 1


def irrep_of(blocks, index):
    bounds = jnp.cumsum(blocks)[:-1]
    return jnp.sum((index[:, None] >= bounds[None, :]).astype(jnp.int32), axis=1)


def shards(
    amplitudes,
    ladder_ints,
    cycle_amps,
    cycle_ints,
    occ_blocks,
    virt_blocks,
    occ_start,
    virt_start,
    eps_occ,
    eps_virt,
):
    i_win = I_DEV * lax.axis_size("opair")
    a_win = A_DEV * lax.axis_size("vpair")
    slab_depth = ladder_ints.shape[0] * ladder_ints.shape[1]
    jb_dev = cycle_ints.shape[2]
    cycle = lax.dot_general(
        cycle_amps, cycle_ints, (((0, 1), (0, 1)), ((), ())), preferred_element_type=jnp.float32
    )
    cycle_part = cycle.reshape(i_win, a_win, jb_dev)
    cycle = lax.psum_scatter(cycle_part, "opair", scatter_dimension=0, tiled=True)
    cycle = lax.all_to_all(cycle, "vpair", split_axis=1, concat_axis=2, tiled=True)
    c_dev = ladder_ints.shape[0]
    v_slab = ladder_ints.reshape(c_dev, ladder_ints.shape[1], A_DEV * NV)
    piece = lax.all_gather(amplitudes, "vpair", axis=0, tiled=True)
    ladder = lax.dot_general(
        piece, v_slab, (((1, 2), (0, 1)), ((), ())), preferred_element_type=jnp.float32
    )
    ladder = ladder.reshape(i_win, NO, A_DEV * NV)
    ladder, cycle = lax.optimization_barrier((ladder, cycle))
    ladder = lax.psum_scatter(ladder, "opair", scatter_dimension=0, tiled=True)
    resid = ladder.reshape(I_DEV, NO, A_DEV, NV).transpose(0, 2, 1, 3) + cycle.reshape(
        I_DEV, A_DEV, NO, NV
    )
    first_occ = occ_start[0] + lax.axis_index("opair") * I_DEV
    first_virt = virt_start[0] + lax.axis_index("vpair") * A_DEV
    glob_i = first_occ + jnp.arange(I_DEV, dtype=jnp.int32)
    glob_a = first_virt + jnp.arange(A_DEV, dtype=jnp.int32)
    sym_i = irrep_of(occ_blocks, glob_i)
    sym_a = irrep_of(virt_blocks, glob_a)
    sym_j = irrep_of(occ_blocks, jnp.arange(NO, dtype=jnp.int32))
    sym_b = irrep_of(virt_blocks, jnp.arange(NV, dtype=jnp.int32))
    total_sym = jnp.bitwise_xor(
        jnp.bitwise_xor(sym_i[:, None, None, None], sym_a[None, :, None, None]),
        jnp.bitwise_xor(sym_j[None, None, :, None], sym_b[None, None, None, :]),
    )
    e_i = lax.dynamic_slice_in_dim(eps_occ, first_occ, I_DEV)
    e_a = lax.dynamic_slice_in_dim(eps_virt, first_virt, A_DEV)
    denom = (
        e_i[:, None, None, None]
        - e_a[None, :, None, None]
        + eps_occ[None, None, :, None]
        - eps_virt[None, None, None, :]
    )
    return jnp.where(total_sym == 0, resid / denom, jnp.float32(0.0))


def solution(mesh):
    placed = (
        P("vpair", "opair", None),
        P("opair", None, "vpair", None),
        P("opair", None, None),
        P("opair", None, "vpair"),
        P(),
        P(),
        P(),
        P(),
        P(),
        P(),
    )
    return jax.shard_map(
        shards,
        mesh=mesh,
        in_specs=placed,
        out_specs=P("opair", "vpair", None, None),
        check_vma=False,
    )
```

```python
import jax
import jax.numpy as jnp
from jax import lax
from jax.sharding import PartitionSpec as P

NO = 100
NV = 1000
I_DEV = 2
A_DEV = 1


def irrep_of(blocks, index):
    bounds = jnp.cumsum(blocks)[:-1]
    return jnp.sum((index[:, None] >= bounds[None, :]).astype(jnp.int32), axis=1)


def shards(
    amplitudes,
    ladder_ints,
    cycle_amps,
    cycle_ints,
    occ_blocks,
    virt_blocks,
    occ_start,
    virt_start,
    eps_occ,
    eps_virt,
):
    i_win = I_DEV * lax.axis_size("opair")
    a_win = A_DEV * lax.axis_size("vpair")
    slab_depth = ladder_ints.shape[0] * ladder_ints.shape[1]
    jb_dev = cycle_ints.shape[2]
    amps_rows = amplitudes.reshape(amplitudes.shape[0], slab_depth)
    amps_rows, cycle_amps = lax.optimization_barrier((amps_rows, cycle_amps))
    cycle = lax.dot_general(
        cycle_amps, cycle_ints, (((0, 1), (0, 1)), ((), ())), preferred_element_type=jnp.float32
    )
    cycle_part = cycle.reshape(i_win, a_win, jb_dev)
    cycle = lax.psum_scatter(cycle_part, "opair", scatter_dimension=0, tiled=True)
    cycle = lax.all_to_all(cycle, "vpair", split_axis=1, concat_axis=2, tiled=True)
    v_flat = ladder_ints.reshape(slab_depth, A_DEV * NV)
    piece = lax.all_gather(
        amps_rows, "vpair", axis=0, tiled=True
    )
    ladder = jnp.dot(piece, v_flat, preferred_element_type=jnp.float32)
    ladder = ladder.reshape(i_win, NO, A_DEV * NV)
    ladder, cycle = lax.optimization_barrier((ladder, cycle))
    ladder = lax.psum_scatter(ladder, "opair", scatter_dimension=0, tiled=True)
    resid = ladder.reshape(I_DEV, NO, A_DEV, NV).transpose(0, 2, 1, 3) + cycle.reshape(
        I_DEV, A_DEV, NO, NV
    )
    first_occ = occ_start[0] + lax.axis_index("opair") * I_DEV
    first_virt = virt_start[0] + lax.axis_index("vpair") * A_DEV
    glob_i = first_occ + jnp.arange(I_DEV, dtype=jnp.int32)
    glob_a = first_virt + jnp.arange(A_DEV, dtype=jnp.int32)
    sym_i = irrep_of(occ_blocks, glob_i)
    sym_a = irrep_of(virt_blocks, glob_a)
    sym_j = irrep_of(occ_blocks, jnp.arange(NO, dtype=jnp.int32))
    sym_b = irrep_of(virt_blocks, jnp.arange(NV, dtype=jnp.int32))
    total_sym = jnp.bitwise_xor(
        jnp.bitwise_xor(sym_i[:, None, None, None], sym_a[None, :, None, None]),
        jnp.bitwise_xor(sym_j[None, None, :, None], sym_b[None, None, None, :]),
    )
    e_i = lax.dynamic_slice_in_dim(eps_occ, first_occ, I_DEV)
    e_a = lax.dynamic_slice_in_dim(eps_virt, first_virt, A_DEV)
    denom = (
        e_i[:, None, None, None]
        - e_a[None, :, None, None]
        + eps_occ[None, None, :, None]
        - eps_virt[None, None, None, :]
    )
    return jnp.where(total_sym == 0, resid / denom, jnp.float32(0.0))


def solution(mesh):
    placed = (
        P("vpair", "opair", None),
        P("opair", None, "vpair", None),
        P("opair", None, None),
        P("opair", None, "vpair"),
        P(),
        P(),
        P(),
        P(),
        P(),
        P(),
    )

    return jax.shard_map(
        shards,
        mesh=mesh,
        in_specs=placed,
        out_specs=P("opair", "vpair", None, None),
        check_vma=False,
    )
```

```python
import jax
import jax.numpy as jnp
from jax import lax
from jax.sharding import PartitionSpec as P

NO = 100
NV = 1000
I_DEV = 2
A_DEV = 1


def irrep_of(blocks, index):
    bounds = jnp.cumsum(blocks)[:-1]
    return jnp.sum((index[:, None] >= bounds[None, :]).astype(jnp.int32), axis=1)


def shards(
    amplitudes,
    ladder_ints,
    cycle_amps,
    cycle_ints,
    occ_blocks,
    virt_blocks,
    occ_start,
    virt_start,
    eps_occ,
    eps_virt,
):
    i_win = I_DEV * lax.axis_size("opair")
    a_win = A_DEV * lax.axis_size("vpair")
    slab_depth = ladder_ints.shape[0] * ladder_ints.shape[1]
    jb_dev = cycle_ints.shape[2]
    amps_rows = amplitudes.reshape(amplitudes.shape[0], slab_depth)
    amps_rows, cycle_amps = lax.optimization_barrier((amps_rows, cycle_amps))
    cycle = lax.dot_general(
        cycle_amps, cycle_ints, (((0, 1), (0, 1)), ((), ())), preferred_element_type=jnp.float32
    )
    cycle_part = cycle.reshape(i_win, a_win, jb_dev)
    cycle = lax.psum_scatter(cycle_part, "opair", scatter_dimension=0, tiled=True)
    v_flat = ladder_ints.reshape(slab_depth, A_DEV * NV)
    piece = lax.all_gather(amps_rows, "vpair", axis=0, tiled=False)
    ladder = lax.dot_general(
        piece, v_flat, (((2,), (0,)), ((), ())), preferred_element_type=jnp.float32
    )
    ladder, cycle = lax.optimization_barrier((ladder, cycle))
    ladder = lax.psum_scatter(ladder, "opair", scatter_dimension=0, tiled=True)
    cycle = lax.all_to_all(cycle, "vpair", split_axis=1, concat_axis=2, tiled=True)
    ladder = ladder.reshape(I_DEV, NO, A_DEV * NV)
    resid = ladder.reshape(I_DEV, NO, A_DEV, NV).transpose(0, 2, 1, 3) + cycle.reshape(
        I_DEV, A_DEV, NO, NV
    )
    first_occ = occ_start[0] + lax.axis_index("opair") * I_DEV
    first_virt = virt_start[0] + lax.axis_index("vpair") * A_DEV
    glob_i = first_occ + jnp.arange(I_DEV, dtype=jnp.int32)
    glob_a = first_virt + jnp.arange(A_DEV, dtype=jnp.int32)
    sym_i = irrep_of(occ_blocks, glob_i)
    sym_a = irrep_of(virt_blocks, glob_a)
    sym_j = irrep_of(occ_blocks, jnp.arange(NO, dtype=jnp.int32))
    sym_b = irrep_of(virt_blocks, jnp.arange(NV, dtype=jnp.int32))
    total_sym = jnp.bitwise_xor(
        jnp.bitwise_xor(sym_i[:, None, None, None], sym_a[None, :, None, None]),
        jnp.bitwise_xor(sym_j[None, None, :, None], sym_b[None, None, None, :]),
    )
    e_i = lax.dynamic_slice_in_dim(eps_occ, first_occ, I_DEV)
    e_a = lax.dynamic_slice_in_dim(eps_virt, first_virt, A_DEV)
    denom = (
        e_i[:, None, None, None]
        - e_a[None, :, None, None]
        + eps_occ[None, None, :, None]
        - eps_virt[None, None, None, :]
    )
    return jnp.where(total_sym == 0, resid / denom, jnp.float32(0.0))


def solution(mesh):
    placed = (
        P("vpair", "opair", None),
        P("opair", None, "vpair", None),
        P("opair", None, None),
        P("opair", None, "vpair"),
        P(),
        P(),
        P(),
        P(),
        P(),
        P(),
    )

    return jax.shard_map(
        shards,
        mesh=mesh,
        in_specs=placed,
        out_specs=P("opair", "vpair", None, None),
        check_vma=False,
    )
```

```python
import jax
import jax.numpy as jnp
from jax import lax
from jax.sharding import PartitionSpec as P

NO = 100
NV = 1000
I_DEV = 2
A_DEV = 1


def irrep_of(blocks, index):
    bounds = jnp.cumsum(blocks)[:-1]
    return jnp.sum((index[:, None] >= bounds[None, :]).astype(jnp.int32), axis=1)


def shards(
    amplitudes,
    ladder_ints,
    cycle_amps,
    cycle_ints,
    occ_blocks,
    virt_blocks,
    occ_start,
    virt_start,
    eps_occ,
    eps_virt,
):
    i_win = I_DEV * lax.axis_size("opair")
    a_win = A_DEV * lax.axis_size("vpair")
    slab_depth = ladder_ints.shape[0] * ladder_ints.shape[1]
    jb_dev = cycle_ints.shape[2]
    amps_rows = amplitudes.reshape(amplitudes.shape[0], slab_depth)
    amps_rows, cycle_amps = lax.optimization_barrier((amps_rows, cycle_amps))
    cycle = lax.dot_general(
        cycle_amps, cycle_ints, (((0, 1), (0, 1)), ((), ())), preferred_element_type=jnp.float32
    )
    cycle_part = cycle.reshape(i_win, a_win, jb_dev)
    cycle = lax.psum_scatter(cycle_part, "opair", scatter_dimension=0, tiled=True)
    v_flat = ladder_ints.reshape(slab_depth, A_DEV * NV)
    piece = lax.all_gather(amps_rows, "vpair", axis=0, tiled=False)
    ladder = lax.dot_general(
        piece, v_flat, (((2,), (0,)), ((), ())), preferred_element_type=jnp.float32
    )
    ladder, cycle = lax.optimization_barrier((ladder, cycle))
    ladder = lax.psum_scatter(ladder, "opair", scatter_dimension=0, tiled=True)
    cycle = lax.all_to_all(cycle, "vpair", split_axis=1, concat_axis=2, tiled=True)
    n_blk, n_row = ladder.shape[0], ladder.shape[1]
    resid = ladder + cycle.reshape(n_blk, n_row, NV)
    first_occ = occ_start[0] + lax.axis_index("opair") * I_DEV
    first_virt = virt_start[0] + lax.axis_index("vpair") * A_DEV
    glob_i = first_occ + jnp.arange(I_DEV, dtype=jnp.int32)
    glob_a = first_virt + jnp.arange(A_DEV, dtype=jnp.int32)
    per_i = n_blk // I_DEV
    sym_i = jnp.repeat(irrep_of(occ_blocks, glob_i), per_i)
    sym_a = irrep_of(virt_blocks, glob_a)
    sym_j = jnp.tile(irrep_of(occ_blocks, jnp.arange(NO, dtype=jnp.int32)).reshape(per_i, n_row), (I_DEV, 1))
    sym_b = irrep_of(virt_blocks, jnp.arange(NV, dtype=jnp.int32))
    total_sym = jnp.bitwise_xor(
        jnp.bitwise_xor(sym_i[:, None, None], sym_a[0]),
        jnp.bitwise_xor(sym_j[:, :, None], sym_b[None, None, :]),
    )
    e_i = jnp.repeat(lax.dynamic_slice_in_dim(eps_occ, first_occ, I_DEV), per_i)
    e_a = lax.dynamic_slice_in_dim(eps_virt, first_virt, A_DEV)
    e_j = jnp.tile(eps_occ.reshape(per_i, n_row), (I_DEV, 1))
    denom = e_i[:, None, None] - e_a[0] + e_j[:, :, None] - eps_virt[None, None, :]
    update = jnp.where(total_sym == 0, resid / denom, jnp.float32(0.0))
    return update.reshape(I_DEV, A_DEV, NO, NV)


def solution(mesh):
    placed = (
        P("vpair", "opair", None),
        P("opair", None, "vpair", None),
        P("opair", None, None),
        P("opair", None, "vpair"),
        P(),
        P(),
        P(),
        P(),
        P(),
        P(),
    )

    return jax.shard_map(
        shards,
        mesh=mesh,
        in_specs=placed,
        out_specs=P("opair", "vpair", None, None),
        check_vma=False,
    )
```
